256 devices in a mesh: space: 64 (over x, z, core), tm: 4 (over y).
Axes of the slice: x: 4, y: 4, z: 8, core: 2. Of those that a mesh axis runs over, the one named last changes fastest.
Arguments:
- snapshots: float32 [4608, 65536], P('tm', 'space'), as said below
- block_starts: int32 [32], P('tm'), may hold values from 0 to 4352, as said below
- owner: int32 [9], replicated, may hold values from 0 to 3, as said below
Outputs:
- modes: float32 [20, 32, 2, 65536], P('tm', None, None, 'space')
The draws below stay inside these ranges and needn't reach their ends.
Inputs may be any that keep to these rules, and one draw needn't show every extreme that they name: `block_starts`: block k lies inside the snapshots held by index k // 8 of tm: its start is that range's first snapshot plus an even offset of 0 to 896; within one range the starts rise with k by 112 or more, the range's first block starts at offset 0 and its last at 896. `owner`: one index of tm owns exactly 5 frequencies, every other index owns one or more and fewer than 5. `snapshots`: finite real values.
All inputs are finite; a program needn't handle non-finite values.
Results may differ from the reference program's by a relative error of at most 0.0003.
Values sent between devices are 32-bit elements; how exact they have to be, the bound alone decides.
No kernel may reach another device: no remote copies, remote signals or barrier semaphores. Data moves between devices by JAX's collectives and lax.ppermute only.
A program may use at most 64 MiB of HBM per device.

```python
import jax
import jax.numpy as jnp
from jax import lax

NFFT = 256
NF = 9
BLK_DEV = 8
NB = 32
TSEG = 1152
TIME = 4608
NPTS = 65536
FCAP = 5
N_TM = 4


def draw_snapshots(key, part):
    key_scale, key_noise, key_time, key_space = jax.random.split(key, 4)
    places = jnp.arange(NPTS, dtype=jnp.float32)
    ramp = 1.0 + 2.0 * places / NPTS
    uniform_draw = jax.random.uniform(key_scale, (NPTS,), jnp.float32)
    scales = jnp.exp(uniform_draw * jnp.log(10.0)) * ramp
    noise = jnp.clip(jax.random.normal(key_noise, (TIME, NPTS), jnp.float32), -4.0, 4.0)
    strength = 240.0
    signal = jnp.clip(jax.random.normal(key_time, (TIME,), jnp.float32), -4.0, 4.0)
    shape_field = jnp.clip(jax.random.normal(key_space, (NPTS,), jnp.float32), -4.0, 4.0)
    values = scales[None, :] * (noise + strength * signal[:, None] * shape_field[None, :])
    return values.astype(jnp.float32)


def draw_block_starts(key, part):
    shard_total = NB // BLK_DEV
    least_gap = 112
    gap_total = BLK_DEV - 1
    slack_half = (TSEG - NFFT - least_gap * gap_total) // 2
    pool = slack_half + gap_total - 1
    shard_keys = jax.random.split(key, shard_total)

    def draw_shard(shard_key):
        cuts = jnp.sort(jax.random.permutation(shard_key, pool)[:gap_total - 1].astype(jnp.int32))
        bounds = jnp.concatenate([jnp.full((1,), -1, jnp.int32), cuts, jnp.full((1,), pool, jnp.int32)])
        extra = bounds[1:] - bounds[:-1] - 1
        gaps = least_gap + 2 * extra
        return jnp.concatenate([jnp.zeros((1,), jnp.int32), jnp.cumsum(gaps).astype(jnp.int32)])
    local_starts = jax.vmap(draw_shard)(shard_keys)
    shifts = TSEG * jnp.arange(shard_total, dtype=jnp.int32)
    return (local_starts + shifts[:, None]).reshape(-1).astype(jnp.int32)


def draw_owner(key, part):
    shard_total = NB // BLK_DEV
    key_busy, key_order, key_rest = jax.random.split(key, 3)
    busiest = jax.random.randint(key_busy, (), 0, shard_total, dtype=jnp.int32)
    freq_order = jax.random.permutation(key_order, NF)
    extra = NF - FCAP - (shard_total - 1)
    offsets = jnp.concatenate([jnp.zeros((FCAP,), jnp.int32), jnp.arange(1, shard_total, dtype=jnp.int32), jax.random.randint(key_rest, (extra,), 1, shard_total, dtype=jnp.int32)])
    devices = (busiest + offsets) % shard_total
    owners = jnp.zeros((NF,), jnp.int32).at[freq_order].set(devices)
    return owners.astype(jnp.int32)


def setup_inputs(seed: int = 0) -> dict:
    streams_of = jax.random.split(jax.random.key(seed), 4)
    snapshots = draw_snapshots(jax.random.fold_in(streams_of[3], 71), 0)
    block_starts = draw_block_starts(jax.random.fold_in(streams_of[3], 71), 0)
    owner = draw_owner(jax.random.fold_in(streams_of[3], 71), 0)
    return dict(snapshots=snapshots, block_starts=block_starts, owner=owner)


def dft_table():
    times = jnp.arange(NFFT, dtype=jnp.int32)
    freqs = jnp.arange(NF, dtype=jnp.int32)
    phase = freqs[:, None] * times[None, :] % NFFT
    angle = 2.0 * jnp.pi / NFFT * phase.astype(jnp.float32)
    window = 0.5 - 0.5 * jnp.cos(2.0 * jnp.pi / NFFT * times.astype(jnp.float32))
    table = jnp.stack([window * jnp.cos(angle), -window * jnp.sin(angle)], axis=1)
    return table.reshape(2 * NF, NFFT)

def orth_pass(matrix, rows_total):
    gram = jnp.dot(matrix, matrix.T, precision=lax.Precision.HIGHEST) / rows_total
    factor = jnp.linalg.cholesky(gram)
    identity = jnp.eye(matrix.shape[0], dtype=matrix.dtype)
    inverse = jax.scipy.linalg.solve_triangular(factor, identity, lower=True)
    return jnp.dot(inverse, matrix, precision=lax.Precision.HIGHEST)

def reference(snapshots, block_starts, owner):
    table = dft_table()
    rows_total = 2.0 * NPTS
    collected = []
    for block in range(NB):
        segment = lax.dynamic_slice_in_dim(snapshots, block_starts[block].astype(jnp.int32), NFFT, 0)
        spectrum = jnp.dot(table, segment, precision=lax.Precision.HIGHEST)
        collected.append(spectrum.reshape(NF, 2 * NPTS))
    spectra = jnp.stack(collected)
    freq_ids = jnp.arange(NF, dtype=jnp.int32)
    modes = jnp.zeros((N_TM * FCAP, NB, 2 * NPTS), jnp.float32)
    for freq in range(NF):
        matrix = spectra[:, freq]
        basis = orth_pass(orth_pass(matrix, rows_total), rows_total)
        same_before = (owner == owner[freq]) & (freq_ids < freq)
        rank_in = jnp.sum(same_before.astype(jnp.int32)).astype(jnp.int32)
        slot_of = (owner[freq].astype(jnp.int32) * FCAP + rank_in).astype(jnp.int32)
        modes = lax.dynamic_update_slice(modes, basis[None].astype(modes.dtype), (slot_of, jnp.int32(0), jnp.int32(0)))
    return modes.reshape(N_TM * FCAP, NB, 2, NPTS)
```

```python
import jax
import jax.numpy as jnp
from jax import lax
from jax.sharding import PartitionSpec as P

NFFT = 256
NF = 9
FCAP = 5


def dft_table():
    times = jnp.arange(NFFT, dtype=jnp.int32)
    freqs = jnp.arange(NF, dtype=jnp.int32)
    phase = freqs[:, None] * times[None, :] % NFFT
    angle = 2.0 * jnp.pi / NFFT * phase.astype(jnp.float32)
    window = 0.5 - 0.5 * jnp.cos(2.0 * jnp.pi / NFFT * times.astype(jnp.float32))
    return jnp.stack([window * jnp.cos(angle), -window * jnp.sin(angle)], axis=1)


def slot_selector(owner, slot_count):
    freq_ids = jnp.arange(owner.shape[0], dtype=jnp.int32)
    before = (owner[None, :] == owner[:, None]) & (freq_ids[None, :] < freq_ids[:, None])
    rank_in = jnp.sum(before.astype(jnp.int32), axis=1)
    slot_of = owner * FCAP + rank_in
    targets = jnp.arange(slot_count, dtype=jnp.int32)
    return (slot_of[None, :] == targets[:, None]).astype(jnp.float32)


def partial_gram(matrices):
    return jnp.einsum("kip,kjp->kij", matrices, matrices, precision=lax.Precision.HIGHEST)


def finish_pass(matrices, totals, rows_total):
    gram = totals / rows_total
    identity = jnp.eye(gram.shape[-1], dtype=jnp.float32)
    diagonal_sum = jnp.trace(gram, axis1=1, axis2=2)
    gram = gram + jnp.where(diagonal_sum == 0.0, 1.0, 0.0)[:, None, None] * identity
    factor = jnp.linalg.cholesky(gram)
    inverse = jax.scipy.linalg.solve_triangular(
        factor, jnp.broadcast_to(identity, gram.shape), lower=True
    )
    return jnp.einsum("kij,kjp->kip", inverse, matrices, precision=lax.Precision.HIGHEST)


def reduce_space(values):
    count = lax.axis_size("space")
    if count & (count - 1):
        return lax.psum(values, "space")
    distance = 1
    while distance < count:
        pairs = [(index, index ^ distance) for index in range(count)]
        values = values + lax.ppermute(values, "space", pairs)
        distance *= 2
    return values


def local(snapshots, block_starts, owner):
    table = dft_table()
    samples, points = snapshots.shape
    block_count = block_starts.shape[0]
    tm_count = lax.axis_size("tm")
    space_count = lax.axis_size("space")
    rows_total = 2.0 * points * space_count
    column_count = block_count * tm_count
    offset = lax.axis_index("tm") * samples
    segments = jnp.stack(
        [
            lax.dynamic_slice_in_dim(snapshots, block_starts[block] - offset, NFFT, 0)
            for block in range(block_count)
        ]
    )
    spectra = jnp.einsum("fct,btp->fbcp", table, segments, precision=lax.Precision.HIGHEST)
    selector = slot_selector(owner, tm_count * FCAP)
    outgoing = jnp.einsum("lf,fbcp->lbcp", selector, spectra, precision=lax.Precision.HIGHEST)
    outgoing = outgoing.reshape(tm_count, FCAP, block_count, 2, points)
    received = lax.all_to_all(outgoing, "tm", split_axis=0, concat_axis=2, tiled=True)
    count = received.shape[1]
    matrices = received[0].reshape(count, column_count, 2 * points)
    for turn in range(2):
        partial_sums = partial_gram(matrices)
        totals = reduce_space(partial_sums)
        matrices = finish_pass(matrices, totals, rows_total)
    return matrices.reshape(count, column_count, 2, points)


def solution(mesh):
    placed = (P("tm", "space"), P("tm"), P())
    return jax.shard_map(
        local, mesh=mesh, in_specs=placed, out_specs=P("tm", None, None, "space"), check_vma=False
    )
```

```python
import functools

import jax
import jax.numpy as jnp
from jax import lax
from jax.experimental import pallas as pl
from jax.experimental.pallas import tpu as pltpu
from jax.sharding import PartitionSpec as P

NFFT = 256
NF = 9
FCAP = 5


def dft_table():
    times = jnp.arange(NFFT, dtype=jnp.int32)
    freqs = jnp.arange(NF, dtype=jnp.int32)
    phase = freqs[:, None] * times[None, :] % NFFT
    angle = 2.0 * jnp.pi / NFFT * phase.astype(jnp.float32)
    window = 0.5 - 0.5 * jnp.cos(2.0 * jnp.pi / NFFT * times.astype(jnp.float32))
    return jnp.stack([window * jnp.cos(angle), -window * jnp.sin(angle)], axis=1)


def windowed_spectra(snapshots, starts):
    samples = snapshots.shape[0]
    lag = jnp.arange(samples, dtype=jnp.int32)[None, :] - starts[:, None]
    inside = (lag >= 0) & (lag < NFFT)
    times = jnp.clip(lag, 0, NFFT - 1)
    freqs = jnp.arange(NF, dtype=jnp.int32)
    phase = freqs[:, None, None] * times[None] % NFFT
    angle = 2.0 * jnp.pi / NFFT * phase.astype(jnp.float32)
    window = 0.5 - 0.5 * jnp.cos(2.0 * jnp.pi / NFFT * times.astype(jnp.float32))
    placed = jnp.stack([window * jnp.cos(angle), -window * jnp.sin(angle)], axis=2)
    placed = jnp.where(inside[None, :, None, :], placed, 0.0)
    return jnp.einsum("fbcs,sp->fbcp", placed, snapshots, precision=lax.Precision.HIGHEST)


def slot_selector(owner, slot_count):
    freq_ids = jnp.arange(owner.shape[0], dtype=jnp.int32)
    before = (owner[None, :] == owner[:, None]) & (freq_ids[None, :] < freq_ids[:, None])
    rank_in = jnp.sum(before.astype(jnp.int32), axis=1)
    slot_of = owner * FCAP + rank_in
    targets = jnp.arange(slot_count, dtype=jnp.int32)
    return (slot_of[None, :] == targets[:, None]).astype(jnp.float32)


def partial_gram(matrices):
    return jnp.einsum("kip,kjp->kij", matrices, matrices, precision=lax.Precision.HIGHEST)


def _inverse_factor_kernel(totals_ref, out_ref, *, rows_total):
    gram = totals_ref[...] / rows_total
    batch, size, _ = gram.shape
    row = lax.broadcasted_iota(jnp.int32, gram.shape, 1)
    col = lax.broadcasted_iota(jnp.int32, gram.shape, 2)
    diagonal = row == col
    trace = jnp.sum(jnp.sum(jnp.where(diagonal, gram, 0.0), axis=2, keepdims=True), axis=1, keepdims=True)
    gram = gram + jnp.where(trace == 0.0, 1.0, 0.0) * diagonal.astype(jnp.float32)
    row_of = lax.broadcasted_iota(jnp.int32, (batch, size, 1), 1)
    col_of = lax.broadcasted_iota(jnp.int32, (batch, 1, size), 2)

    def step(j, carry):
        schur, elim, pivots = carry
        column = jnp.sum(jnp.where(col == j, schur, 0.0), axis=2, keepdims=True)
        pivot_row = jnp.sum(jnp.where(row == j, schur, 0.0), axis=1, keepdims=True)
        elim_row = jnp.sum(jnp.where(row == j, elim, 0.0), axis=1, keepdims=True)
        pivot = jnp.sum(jnp.where(col_of == j, pivot_row, 0.0), axis=2, keepdims=True)
        factor = jnp.where(row_of > j, column / pivot, 0.0)
        schur = schur - factor * pivot_row
        elim = elim - factor * elim_row
        pivots = jnp.where(row_of == j, pivot, pivots)
        return schur, elim, pivots

    start = (gram, diagonal.astype(jnp.float32), jnp.ones((batch, size, 1), jnp.float32))
    _, elim, pivots = lax.fori_loop(0, size, step, start)
    out_ref[...] = elim / jnp.sqrt(pivots)


def inverse_factor(totals, rows_total):
    return pl.pallas_call(
        functools.partial(_inverse_factor_kernel, rows_total=rows_total),
        out_shape=jax.ShapeDtypeStruct(totals.shape, jnp.float32),
        in_specs=[pl.BlockSpec(memory_space=pltpu.VMEM)],
        out_specs=pl.BlockSpec(memory_space=pltpu.VMEM),
    )(totals)


def finish_pass(matrices, totals, rows_total):
    inverse = inverse_factor(totals, rows_total)
    return jnp.einsum("kij,kjp->kip", inverse, matrices, precision=lax.Precision.HIGHEST)


def reduce_space(values):
    count = lax.axis_size("space")
    radix = 4
    distance = 1
    while distance < count:
        width = min(radix, count // distance)
        leaves = [values]
        for step in range(1, width):
            pairs = [(index, index ^ (step * distance)) for index in range(count)]
            leaves.append(lax.ppermute(values, "space", pairs))
        while len(leaves) > 1:
            leaves = [leaves[i] + leaves[i + 1] for i in range(0, len(leaves), 2)]
        values = leaves[0]
        distance *= width
    return values


def local(snapshots, block_starts, owner):
    table = dft_table()
    samples, points = snapshots.shape
    block_count = block_starts.shape[0]
    tm_count = lax.axis_size("tm")
    space_count = lax.axis_size("space")
    rows_total = 2.0 * points * space_count
    column_count = block_count * tm_count
    offset = lax.axis_index("tm") * samples
    spectra = windowed_spectra(snapshots, block_starts - offset)
    selector = slot_selector(owner, tm_count * FCAP)
    outgoing = jnp.einsum("lf,fbcp->lbcp", selector, spectra, precision=lax.Precision.HIGHEST)
    outgoing = outgoing.reshape(tm_count, FCAP, block_count, 2, points)
    received = lax.all_to_all(outgoing, "tm", split_axis=0, concat_axis=2, tiled=True)
    count = received.shape[1]
    matrices = received[0].reshape(count, column_count, 2 * points)
    for turn in range(2):
        partial_sums = partial_gram(matrices)
        totals = reduce_space(partial_sums)
        matrices = finish_pass(matrices, totals, rows_total)
    return matrices.reshape(count, column_count, 2, points)


def solution(mesh):
    placed = (P("tm", "space"), P("tm"), P())
    return jax.shard_map(
        local, mesh=mesh, in_specs=placed, out_specs=P("tm", None, None, "space"), check_vma=False
    )
```

```python
import functools

import jax
import jax.numpy as jnp
from jax import lax
from jax.experimental import pallas as pl
from jax.experimental.pallas import tpu as pltpu
from jax.sharding import PartitionSpec as P

NFFT = 256
NF = 9
FCAP = 5


def dft_table():
    times = jnp.arange(NFFT, dtype=jnp.int32)
    freqs = jnp.arange(NF, dtype=jnp.int32)
    phase = freqs[:, None] * times[None, :] % NFFT
    angle = 2.0 * jnp.pi / NFFT * phase.astype(jnp.float32)
    window = 0.5 - 0.5 * jnp.cos(2.0 * jnp.pi / NFFT * times.astype(jnp.float32))
    return jnp.stack([window * jnp.cos(angle), -window * jnp.sin(angle)], axis=1)


def windowed_spectra(snapshots, starts):
    samples = snapshots.shape[0]
    lag = jnp.arange(samples, dtype=jnp.int32)[None, :] - starts[:, None]
    inside = (lag >= 0) & (lag < NFFT)
    times = jnp.clip(lag, 0, NFFT - 1)
    freqs = jnp.arange(NF, dtype=jnp.int32)
    phase = freqs[:, None, None] * times[None] % NFFT
    angle = 2.0 * jnp.pi / NFFT * phase.astype(jnp.float32)
    window = 0.5 - 0.5 * jnp.cos(2.0 * jnp.pi / NFFT * times.astype(jnp.float32))
    placed = jnp.stack([window * jnp.cos(angle), -window * jnp.sin(angle)], axis=2)
    placed = jnp.where(inside[None, :, None, :], placed, 0.0)
    return jnp.einsum("fbcs,sp->fbcp", placed, snapshots, precision=lax.Precision.HIGHEST)


def slot_selector(owner, slot_count):
    freq_ids = jnp.arange(owner.shape[0], dtype=jnp.int32)
    before = (owner[None, :] == owner[:, None]) & (freq_ids[None, :] < freq_ids[:, None])
    rank_in = jnp.sum(before.astype(jnp.int32), axis=1)
    slot_of = owner * FCAP + rank_in
    targets = jnp.arange(slot_count, dtype=jnp.int32)
    return (slot_of[None, :] == targets[:, None]).astype(jnp.float32)


def partial_gram(matrices):
    return jnp.einsum("kip,kjp->kij", matrices, matrices, precision=lax.Precision.HIGHEST)


def _inverse_factor_kernel(totals_ref, out_ref, *, rows_total):
    gram = totals_ref[...] / rows_total
    batch, size, _ = gram.shape
    row = lax.broadcasted_iota(jnp.int32, gram.shape, 1)
    col = lax.broadcasted_iota(jnp.int32, gram.shape, 2)
    diagonal = row == col
    trace = jnp.sum(jnp.sum(jnp.where(diagonal, gram, 0.0), axis=2, keepdims=True), axis=1, keepdims=True)
    gram = gram + jnp.where(trace == 0.0, 1.0, 0.0) * diagonal.astype(jnp.float32)
    row_of = lax.broadcasted_iota(jnp.int32, (batch, size, 1), 1)
    col_of = lax.broadcasted_iota(jnp.int32, (batch, 1, size), 2)

    def step(j, carry):
        schur, elim, pivots = carry
        column = jnp.sum(jnp.where(col == j, schur, 0.0), axis=2, keepdims=True)
        pivot_row = jnp.sum(jnp.where(row == j, schur, 0.0), axis=1, keepdims=True)
        elim_row = jnp.sum(jnp.where(row == j, elim, 0.0), axis=1, keepdims=True)
        pivot = jnp.sum(jnp.where(col_of == j, pivot_row, 0.0), axis=2, keepdims=True)
        factor = jnp.where(row_of > j, column / pivot, 0.0)
        schur = schur - factor * pivot_row
        elim = elim - factor * elim_row
        pivots = jnp.where(row_of == j, pivot, pivots)
        return schur, elim, pivots

    start = (gram, diagonal.astype(jnp.float32), jnp.ones((batch, size, 1), jnp.float32))
    _, elim, pivots = lax.fori_loop(0, size, step, start, unroll=True)
    out_ref[...] = elim / jnp.sqrt(pivots)


def inverse_factor(totals, rows_total):
    return pl.pallas_call(
        functools.partial(_inverse_factor_kernel, rows_total=rows_total),
        out_shape=jax.ShapeDtypeStruct(totals.shape, jnp.float32),
        in_specs=[pl.BlockSpec(memory_space=pltpu.VMEM)],
        out_specs=pl.BlockSpec(memory_space=pltpu.VMEM),
    )(totals)


def finish_pass(matrices, totals, rows_total):
    inverse = inverse_factor(totals, rows_total)
    return jnp.einsum("kij,kjp->kip", inverse, matrices, precision=lax.Precision.HIGHEST)


def reduce_space(values):
    count = lax.axis_size("space")
    radix = 4
    distance = 1
    while distance < count:
        width = min(radix, count // distance)
        leaves = [values]
        for step in range(1, width):
            pairs = [(index, index ^ (step * distance)) for index in range(count)]
            leaves.append(lax.ppermute(values, "space", pairs))
        while len(leaves) > 1:
            leaves = [leaves[i] + leaves[i + 1] for i in range(0, len(leaves), 2)]
        values = leaves[0]
        distance *= width
    return values


def local(snapshots, block_starts, owner):
    table = dft_table()
    samples, points = snapshots.shape
    block_count = block_starts.shape[0]
    tm_count = lax.axis_size("tm")
    space_count = lax.axis_size("space")
    rows_total = 2.0 * points * space_count
    column_count = block_count * tm_count
    offset = lax.axis_index("tm") * samples
    spectra = windowed_spectra(snapshots, block_starts - offset)
    selector = slot_selector(owner, tm_count * FCAP)
    outgoing = jnp.einsum("lf,fbcp->lbcp", selector, spectra, precision=lax.Precision.HIGHEST)
    outgoing = outgoing.reshape(tm_count, FCAP, block_count, 2, points)
    received = lax.all_to_all(outgoing, "tm", split_axis=0, concat_axis=2, tiled=True)
    count = received.shape[1]
    matrices = received[0].reshape(count, column_count, 2 * points)
    for turn in range(2):
        partial_sums = partial_gram(matrices)
        totals = reduce_space(partial_sums)
        matrices = finish_pass(matrices, totals, rows_total)
    return matrices.reshape(count, column_count, 2, points)


def solution(mesh):
    placed = (P("tm", "space"), P("tm"), P())
    return jax.shard_map(
        local, mesh=mesh, in_specs=placed, out_specs=P("tm", None, None, "space"), check_vma=False
    )
```

```python
import functools

import jax
import jax.numpy as jnp
from jax import lax
from jax.experimental import pallas as pl
from jax.experimental.pallas import tpu as pltpu
from jax.sharding import PartitionSpec as P

NFFT = 256
NF = 9
FCAP = 5


def dft_table():
    times = jnp.arange(NFFT, dtype=jnp.int32)
    freqs = jnp.arange(NF, dtype=jnp.int32)
    phase = freqs[:, None] * times[None, :] % NFFT
    angle = 2.0 * jnp.pi / NFFT * phase.astype(jnp.float32)
    window = 0.5 - 0.5 * jnp.cos(2.0 * jnp.pi / NFFT * times.astype(jnp.float32))
    return jnp.stack([window * jnp.cos(angle), -window * jnp.sin(angle)], axis=1)


def windowed_spectra(snapshots, starts):
    samples = snapshots.shape[0]
    lag = jnp.arange(samples, dtype=jnp.int32)[None, :] - starts[:, None]
    inside = (lag >= 0) & (lag < NFFT)
    times = jnp.clip(lag, 0, NFFT - 1)
    freqs = jnp.arange(NF, dtype=jnp.int32)
    phase = freqs[:, None, None] * times[None] % NFFT
    angle = 2.0 * jnp.pi / NFFT * phase.astype(jnp.float32)
    window = 0.5 - 0.5 * jnp.cos(2.0 * jnp.pi / NFFT * times.astype(jnp.float32))
    placed = jnp.stack([window * jnp.cos(angle), -window * jnp.sin(angle)], axis=2)
    placed = jnp.where(inside[None, :, None, :], placed, 0.0)
    return jnp.einsum("fbcs,sp->fbcp", placed, snapshots, precision=lax.Precision.HIGHEST)


def slot_selector(owner, slot_count):
    freq_ids = jnp.arange(owner.shape[0], dtype=jnp.int32)
    before = (owner[None, :] == owner[:, None]) & (freq_ids[None, :] < freq_ids[:, None])
    rank_in = jnp.sum(before.astype(jnp.int32), axis=1)
    slot_of = owner * FCAP + rank_in
    targets = jnp.arange(slot_count, dtype=jnp.int32)
    return (slot_of[None, :] == targets[:, None]).astype(jnp.float32)


def partial_gram(matrices):
    return jnp.einsum("kip,kjp->kij", matrices, matrices, precision=lax.Precision.HIGHEST)


def _inverse_factor_kernel(totals_ref, out_ref, *, rows_total):
    gram = totals_ref[...] / rows_total
    batch, size, _ = gram.shape
    row = lax.broadcasted_iota(jnp.int32, gram.shape, 1)
    col = lax.broadcasted_iota(jnp.int32, gram.shape, 2)
    diagonal = row == col
    trace = jnp.sum(jnp.sum(jnp.where(diagonal, gram, 0.0), axis=2, keepdims=True), axis=1, keepdims=True)
    gram = gram + jnp.where(trace == 0.0, 1.0, 0.0) * diagonal.astype(jnp.float32)
    row_of = lax.broadcasted_iota(jnp.int32, (batch, size, 1), 1)
    col_of = lax.broadcasted_iota(jnp.int32, (batch, 1, size), 2)

    def step(j, carry):
        schur, elim, pivots = carry
        column = jnp.sum(jnp.where(col == j, schur, 0.0), axis=2, keepdims=True)
        pivot_row = jnp.sum(jnp.where(row == j, schur, 0.0), axis=1, keepdims=True)
        elim_row = jnp.sum(jnp.where(row == j, elim, 0.0), axis=1, keepdims=True)
        pivot = jnp.sum(jnp.where(col_of == j, pivot_row, 0.0), axis=2, keepdims=True)
        factor = jnp.where(row_of > j, column / pivot, 0.0)
        schur = schur - factor * pivot_row
        elim = elim - factor * elim_row
        pivots = jnp.where(row_of == j, pivot, pivots)
        return schur, elim, pivots

    start = (gram, diagonal.astype(jnp.float32), jnp.ones((batch, size, 1), jnp.float32))
    _, elim, pivots = lax.fori_loop(0, size, step, start, unroll=True)
    out_ref[...] = elim / jnp.sqrt(pivots)


def inverse_factor(totals, rows_total):
    return pl.pallas_call(
        functools.partial(_inverse_factor_kernel, rows_total=rows_total),
        out_shape=jax.ShapeDtypeStruct(totals.shape, jnp.float32),
        in_specs=[pl.BlockSpec(memory_space=pltpu.VMEM)],
        out_specs=pl.BlockSpec(memory_space=pltpu.VMEM),
    )(totals)


def finish_pass(matrices, totals, rows_total):
    inverse = inverse_factor(totals, rows_total)
    return jnp.einsum("kij,kjp->kip", inverse, matrices, precision=lax.Precision.HIGHEST)


def reduce_space(values):
    count = lax.axis_size("space")
    for masks in [[4, 8, 12], [1, 2, 3], [16, 32, 48]]:
        leaves = [values]
        for mask in masks:
            pairs = [(index, index ^ mask) for index in range(count)]
            leaves.append(lax.ppermute(values, "space", pairs))
        while len(leaves) > 1:
            leaves = [leaves[i] + leaves[i + 1] for i in range(0, len(leaves), 2)]
        values = leaves[0]
    return values


def local(snapshots, block_starts, owner):
    table = dft_table()
    samples, points = snapshots.shape
    block_count = block_starts.shape[0]
    tm_count = lax.axis_size("tm")
    space_count = lax.axis_size("space")
    rows_total = 2.0 * points * space_count
    column_count = block_count * tm_count
    offset = lax.axis_index("tm") * samples
    spectra = windowed_spectra(snapshots, block_starts - offset)
    selector = slot_selector(owner, tm_count * FCAP)
    outgoing = jnp.einsum("lf,fbcp->lbcp", selector, spectra, precision=lax.Precision.HIGHEST)
    outgoing = outgoing.reshape(tm_count, FCAP, block_count, 2, points)
    received = lax.all_to_all(outgoing, "tm", split_axis=0, concat_axis=2, tiled=True)
    count = received.shape[1]
    matrices = received[0].reshape(count, column_count, 2 * points)
    for turn in range(2):
        partial_sums = partial_gram(matrices)
        totals = reduce_space(partial_sums)
        matrices = finish_pass(matrices, totals, rows_total)
    return matrices.reshape(count, column_count, 2, points)


def solution(mesh):
    placed = (P("tm", "space"), P("tm"), P())
    return jax.shard_map(
        local, mesh=mesh, in_specs=placed, out_specs=P("tm", None, None, "space"), check_vma=False
    )
```

```python
import functools

import jax
import jax.numpy as jnp
from jax import lax
from jax.experimental import pallas as pl
from jax.experimental.pallas import tpu as pltpu
from jax.sharding import PartitionSpec as P

NFFT = 256
NF = 9
FCAP = 5


def dft_table():
    times = jnp.arange(NFFT, dtype=jnp.int32)
    freqs = jnp.arange(NF, dtype=jnp.int32)
    phase = freqs[:, None] * times[None, :] % NFFT
    angle = 2.0 * jnp.pi / NFFT * phase.astype(jnp.float32)
    window = 0.5 - 0.5 * jnp.cos(2.0 * jnp.pi / NFFT * times.astype(jnp.float32))
    return jnp.stack([window * jnp.cos(angle), -window * jnp.sin(angle)], axis=1)


def windowed_spectra(snapshots, starts):
    samples = snapshots.shape[0]
    lag = jnp.arange(samples, dtype=jnp.int32)[None, :] - starts[:, None]
    inside = (lag >= 0) & (lag < NFFT)
    times = jnp.clip(lag, 0, NFFT - 1)
    freqs = jnp.arange(NF, dtype=jnp.int32)
    phase = freqs[:, None, None] * times[None] % NFFT
    angle = 2.0 * jnp.pi / NFFT * phase.astype(jnp.float32)
    window = 0.5 - 0.5 * jnp.cos(2.0 * jnp.pi / NFFT * times.astype(jnp.float32))
    placed = jnp.stack([window * jnp.cos(angle), -window * jnp.sin(angle)], axis=2)
    placed = jnp.where(inside[None, :, None, :], placed, 0.0)
    return jnp.einsum("fbcs,sp->fbcp", placed, snapshots, precision=lax.Precision.HIGHEST)


def slot_sources(owner, slot_count):
    freq_ids = jnp.arange(owner.shape[0], dtype=jnp.int32)
    before = (owner[None, :] == owner[:, None]) & (freq_ids[None, :] < freq_ids[:, None])
    rank_in = jnp.sum(before.astype(jnp.int32), axis=1)
    slot_of = owner * FCAP + rank_in
    hits = slot_of[None, :] == jnp.arange(slot_count, dtype=jnp.int32)[:, None]
    chosen = jnp.sum(jnp.where(hits, freq_ids[None, :], 0), axis=1)
    return chosen, jnp.any(hits, axis=1)


def partial_gram(matrices):
    return jnp.einsum("kip,kjp->kij", matrices, matrices, precision=lax.Precision.HIGHEST)


def _inverse_factor_kernel(own_ref, first_ref, second_ref, third_ref, out_ref, *, rows_total):
    totals = (own_ref[...] + first_ref[...]) + (second_ref[...] + third_ref[...])
    gram = totals / rows_total
    batch, size, _ = gram.shape
    row = lax.broadcasted_iota(jnp.int32, gram.shape, 1)
    col = lax.broadcasted_iota(jnp.int32, gram.shape, 2)
    diagonal = row == col
    trace = jnp.sum(jnp.sum(jnp.where(diagonal, gram, 0.0), axis=2, keepdims=True), axis=1, keepdims=True)
    gram = gram + jnp.where(trace == 0.0, 1.0, 0.0) * diagonal.astype(jnp.float32)
    row_of = lax.broadcasted_iota(jnp.int32, (batch, size, 1), 1)
    col_of = lax.broadcasted_iota(jnp.int32, (batch, 1, size), 2)

    def step(j, carry):
        schur, elim, pivots = carry
        column = jnp.sum(jnp.where(col == j, schur, 0.0), axis=2, keepdims=True)
        pivot_row = jnp.sum(jnp.where(row == j, schur, 0.0), axis=1, keepdims=True)
        elim_row = jnp.sum(jnp.where(row == j, elim, 0.0), axis=1, keepdims=True)
        pivot = jnp.sum(jnp.where(col_of == j, pivot_row, 0.0), axis=2, keepdims=True)
        factor = jnp.where(row_of > j, column / pivot, 0.0)
        schur = schur - factor * pivot_row
        elim = elim - factor * elim_row
        pivots = jnp.where(row_of == j, pivot, pivots)
        return schur, elim, pivots

    start = (gram, diagonal.astype(jnp.float32), jnp.ones((batch, size, 1), jnp.float32))
    _, elim, pivots = lax.fori_loop(0, size, step, start, unroll=True)
    out_ref[...] = elim / jnp.sqrt(pivots)


def inverse_factor(leaves, rows_total):
    return pl.pallas_call(
        functools.partial(_inverse_factor_kernel, rows_total=rows_total),
        out_shape=jax.ShapeDtypeStruct(leaves[0].shape, jnp.float32),
        in_specs=[pl.BlockSpec(memory_space=pltpu.VMEM)] * 4,
        out_specs=pl.BlockSpec(memory_space=pltpu.VMEM),
    )(*leaves)


def finish_pass(matrices, leaves, rows_total):
    inverse = inverse_factor(leaves, rows_total)
    return jnp.einsum("kij,kjp->kip", inverse, matrices, precision=lax.Precision.HIGHEST)


def reduce_space(values):
    count = lax.axis_size("space")
    rounds = [[4, 8, 12], [1, 2, 3], [16, 32, 48]]
    for number, masks in enumerate(rounds):
        leaves = [values]
        for mask in masks:
            pairs = [(index, index ^ mask) for index in range(count)]
            leaves.append(lax.ppermute(values, "space", pairs))
        if number == len(rounds) - 1:
            return leaves
        values = (leaves[0] + leaves[1]) + (leaves[2] + leaves[3])


def local(snapshots, block_starts, owner):
    table = dft_table()
    samples, points = snapshots.shape
    block_count = block_starts.shape[0]
    tm_count = lax.axis_size("tm")
    space_count = lax.axis_size("space")
    rows_total = 2.0 * points * space_count
    column_count = block_count * tm_count
    offset = lax.axis_index("tm") * samples
    spectra = windowed_spectra(snapshots, block_starts - offset)
    chosen, filled = slot_sources(owner, tm_count * FCAP)
    outgoing = jnp.where(filled[:, None, None, None], jnp.take(spectra, chosen, axis=0), 0.0)
    outgoing = outgoing.reshape(tm_count, FCAP, block_count, 2, points)
    received = lax.all_to_all(outgoing, "tm", split_axis=0, concat_axis=2, tiled=True)
    count = received.shape[1]
    matrices = received[0].reshape(count, column_count, 2 * points)
    for turn in range(2):
        partial_sums = partial_gram(matrices)
        leaves = reduce_space(partial_sums)
        matrices = finish_pass(matrices, leaves, rows_total)
    return matrices.reshape(count, column_count, 2, points)


def solution(mesh):
    placed = (P("tm", "space"), P("tm"), P())
    return jax.shard_map(
        local, mesh=mesh, in_specs=placed, out_specs=P("tm", None, None, "space"), check_vma=False
    )
```

```python
import functools

import jax
import jax.numpy as jnp
from jax import lax
from jax.experimental import pallas as pl
from jax.experimental.pallas import tpu as pltpu
from jax.sharding import PartitionSpec as P

NFFT = 256
NF = 9
FCAP = 5


def dft_table():
    times = jnp.arange(NFFT, dtype=jnp.int32)
    freqs = jnp.arange(NF, dtype=jnp.int32)
    phase = freqs[:, None] * times[None, :] % NFFT
    angle = 2.0 * jnp.pi / NFFT * phase.astype(jnp.float32)
    window = 0.5 - 0.5 * jnp.cos(2.0 * jnp.pi / NFFT * times.astype(jnp.float32))
    return jnp.stack([window * jnp.cos(angle), -window * jnp.sin(angle)], axis=1)


def windowed_spectra(snapshots, starts):
    samples = snapshots.shape[0]
    lag = jnp.arange(samples, dtype=jnp.int32)[None, :] - starts[:, None]
    inside = (lag >= 0) & (lag < NFFT)
    times = jnp.clip(lag, 0, NFFT - 1)
    freqs = jnp.arange(NF, dtype=jnp.int32)
    phase = freqs[:, None, None] * times[None] % NFFT
    angle = 2.0 * jnp.pi / NFFT * phase.astype(jnp.float32)
    window = 0.5 - 0.5 * jnp.cos(2.0 * jnp.pi / NFFT * times.astype(jnp.float32))
    placed = jnp.stack([window * jnp.cos(angle), -window * jnp.sin(angle)], axis=2)
    placed = jnp.where(inside[None, :, None, :], placed, 0.0)
    return jnp.einsum("fbcs,sp->fbcp", placed, snapshots, precision=lax.Precision.HIGHEST)


def slot_sources(owner, slot_count):
    freq_ids = jnp.arange(owner.shape[0], dtype=jnp.int32)
    before = (owner[None, :] == owner[:, None]) & (freq_ids[None, :] < freq_ids[:, None])
    rank_in = jnp.sum(before.astype(jnp.int32), axis=1)
    slot_of = owner * FCAP + rank_in
    hits = slot_of[None, :] == jnp.arange(slot_count, dtype=jnp.int32)[:, None]
    chosen = jnp.sum(jnp.where(hits, freq_ids[None, :], 0), axis=1)
    return chosen, jnp.any(hits, axis=1)


def partial_gram(matrices):
    return jnp.einsum("kip,kjp->kij", matrices, matrices, precision=lax.Precision.HIGHEST)


def _inverse_factor_kernel(own_ref, first_ref, second_ref, third_ref, out_ref, *, rows_total):
    totals = (own_ref[...] + first_ref[...]) + (second_ref[...] + third_ref[...])
    gram = totals / rows_total
    batch, size, _ = gram.shape
    row = lax.broadcasted_iota(jnp.int32, gram.shape, 1)
    col = lax.broadcasted_iota(jnp.int32, gram.shape, 2)
    diagonal = row == col
    trace = jnp.sum(jnp.sum(jnp.where(diagonal, gram, 0.0), axis=2, keepdims=True), axis=1, keepdims=True)
    gram = gram + jnp.where(trace == 0.0, 1.0, 0.0) * diagonal.astype(jnp.float32)
    row_of = lax.broadcasted_iota(jnp.int32, (batch, size, 1), 1)
    col_of = lax.broadcasted_iota(jnp.int32, (batch, 1, size), 2)

    def step(j, carry):
        schur, elim, pivots = carry
        column = jnp.sum(jnp.where(col == j, schur, 0.0), axis=2, keepdims=True)
        pivot_row = jnp.sum(jnp.where(row == j, schur, 0.0), axis=1, keepdims=True)
        elim_row = jnp.sum(jnp.where(row == j, elim, 0.0), axis=1, keepdims=True)
        pivot = jnp.sum(jnp.where(col_of == j, pivot_row, 0.0), axis=2, keepdims=True)
        factor = jnp.where(row_of > j, column / pivot, 0.0)
        schur = schur - factor * pivot_row
        elim = elim - factor * elim_row
        pivots = jnp.where(row_of == j, pivot, pivots)
        return schur, elim, pivots

    start = (gram, diagonal.astype(jnp.float32), jnp.ones((batch, size, 1), jnp.float32))
    _, elim, pivots = lax.fori_loop(0, size, step, start, unroll=True)
    out_ref[...] = elim / jnp.sqrt(pivots)


def inverse_factor(leaves, rows_total):
    return pl.pallas_call(
        functools.partial(_inverse_factor_kernel, rows_total=rows_total),
        out_shape=jax.ShapeDtypeStruct(leaves[0].shape, jnp.float32),
        in_specs=[pl.BlockSpec(memory_space=pltpu.VMEM)] * 4,
        out_specs=pl.BlockSpec(memory_space=pltpu.VMEM),
    )(*leaves)


def finish_pass(matrices, leaves, rows_total):
    inverse = inverse_factor(leaves, rows_total)
    return jnp.einsum("kij,kjp->kip", inverse, matrices, precision=lax.Precision.HIGHEST)


def reduce_space(values):
    count = lax.axis_size("space")
    rounds = [[8, 4, 12], [2, 1, 3], [32, 16, 48]]
    for number, masks in enumerate(rounds):
        leaves = [values]
        for mask in masks:
            pairs = [(index, index ^ mask) for index in range(count)]
            leaves.append(lax.ppermute(values, "space", pairs))
        if number == len(rounds) - 1:
            return leaves
        values = (leaves[0] + leaves[1]) + (leaves[2] + leaves[3])


def local(snapshots, block_starts, owner):
    table = dft_table()
    samples, points = snapshots.shape
    block_count = block_starts.shape[0]
    tm_count = lax.axis_size("tm")
    space_count = lax.axis_size("space")
    rows_total = 2.0 * points * space_count
    column_count = block_count * tm_count
    offset = lax.axis_index("tm") * samples
    spectra = windowed_spectra(snapshots, block_starts - offset)
    chosen, filled = slot_sources(owner, tm_count * FCAP)
    outgoing = jnp.where(filled[:, None, None, None], jnp.take(spectra, chosen, axis=0), 0.0)
    outgoing = outgoing.reshape(tm_count, FCAP, block_count, 2, points)
    received = lax.all_to_all(outgoing, "tm", split_axis=0, concat_axis=2, tiled=True)
    count = received.shape[1]
    matrices = received[0].reshape(count, column_count, 2 * points)
    for turn in range(2):
        partial_sums = partial_gram(matrices)
        leaves = reduce_space(partial_sums)
        matrices = finish_pass(matrices, leaves, rows_total)
    return matrices.reshape(count, column_count, 2, points)


def solution(mesh):
    placed = (P("tm", "space"), P("tm"), P())
    return jax.shard_map(
        local, mesh=mesh, in_specs=placed, out_specs=P("tm", None, None, "space"), check_vma=False
    )
```
